32 devices in a mesh: slab: 2 (over x), row: 8 (over z, y), col: 2 (over core).
Axes of the slice: x: 2, y: 2, z: 4, core: 2. Of those that a mesh axis runs over, the one named last changes fastest.
Arguments:
- features: bfloat16 [256, 512, 256], P(('slab', 'row'), 'col'), parts along dimension 0, may hold values from -6 to 6
- teacher: bfloat16 [256, 512, 256], P(('slab', 'row'), 'col'), parts along dimension 0, may hold values from -6 to 6
- kernel_horiz: float32 [31, 256], replicated, may hold values from -1 to 1
- kernel_vert: float32 [31, 256], replicated, may hold values from -1 to 1
- norm_gain_vector: float32 [256], replicated, may hold values from 0.25 to 1.75
- weight_in: bfloat16 [256, 1024], replicated, may hold values from -0.375 to 0.375
- weight_out: bfloat16 [1024, 256], replicated, may hold values from -0.1875 to 0.1875
Outputs:
- student: bfloat16 [256, 512, 256], P(('slab', 'row'), 'col'), parts along dimension 0
- grad_features: bfloat16 [256, 512, 256], P(('slab', 'row'), 'col'), parts along dimension 0
- grad_in: float32 [512, 1024], P('slab'), parts along dimension 0
- grad_out: float32 [2048, 256], P('slab'), parts along dimension 0
- grad_horiz: float32 [62, 256], P('slab'), parts along dimension 0
- grad_vert: float32 [62, 256], P('slab'), parts along dimension 0
- gain_gradient: float32 [512], P('slab'), parts along dimension 0
The draws below stay inside these ranges and needn't reach their ends.
There are 2 independent parts, one for each index of `slab`. The reference program is written for one: setup_inputs(seed, part) draws one part's arguments, and reference() takes and returns one part's arrays. A program takes and returns all parts, laid end to end along the dimension named above; an argument that names none is the same for every part. Nothing has to cross between parts.
All inputs are finite; a program needn't handle non-finite values.
Results may differ from the reference program's by a relative error of at most 0.0061.
Values may be sent and summed in bfloat16 or wider, within the bound.
No kernel may reach another device: no remote copies, remote signals or barrier semaphores. Data moves between devices by JAX's collectives and lax.ppermute only.
A program may use at most 128 MiB of HBM per device.

```python
import jax
import jax.numpy as jnp
from jax import lax

C = 256
F = 1024
K = 31
HALF = 15
ROWS_DEV = 16
HEIGHT = 128
WIDTH = 512


def level_of(stream_key, extent, split, low, top_value):
    gain = 1.0
    for position, shards_of in split:
        draws = jax.random.uniform(jax.random.fold_in(jax.random.fold_in(stream_key, 6), position), (shards_of,), jnp.float32, low / len(split), top_value / len(split))
        gain = gain * jnp.repeat(jnp.exp(draws), extent[position] // shards_of).reshape((-1,) + (1,) * (len(extent) - 1 - position))
    return gain


def gaussian(key, shape, scale, most, pieces=(), held_as=jnp.bfloat16):
    array = scale * jax.random.normal(key, shape, jnp.float32)
    if pieces:
        array = array * level_of(key, shape, pieces, -0.22, 0.18)
    return jnp.clip(array, -most, most).astype(held_as)


def setup_inputs(seed: int = 0, part: int = 0) -> dict:
    key_list = jax.random.split(jax.random.key(seed), 8)
    part_splits = jax.random.split(jax.random.fold_in(key_list[7], part), 8)
    features = gaussian(part_splits[0], (HEIGHT, WIDTH, C), 1.0, 6.0, ((0, 8), (1, 2)))
    teacher = gaussian(part_splits[1], (HEIGHT, WIDTH, C), 1.0, 6.0, ((0, 8), (1, 2)))
    kernel_horiz = gaussian(key_list[2], (K, C), K ** -0.5, 1.0, (), jnp.float32)
    kernel_vert = gaussian(key_list[3], (K, C), K ** -0.5, 1.0, (), jnp.float32)
    norm_gain_vector = jnp.clip(1.0 + 0.15 * jax.random.normal(key_list[4], (C,), jnp.float32), 0.25, 1.75)
    weight_in = gaussian(key_list[5], (C, F), C ** -0.5, 0.375)
    weight_out = gaussian(key_list[6], (F, C), F ** -0.5, 0.1875)
    return dict(features=features, teacher=teacher, kernel_horiz=kernel_horiz, kernel_vert=kernel_vert, norm_gain_vector=norm_gain_vector, weight_in=weight_in, weight_out=weight_out)


root_half = 0.7071067811865476
inv_root_two_pi = 0.3989422804014327

def horizontal(padded, kernel, count):
    total = jnp.zeros((padded.shape[0], count, padded.shape[2]), jnp.float32)
    for offset in range(kernel.shape[0]):
        total = total + kernel[offset] * padded[:, offset:offset + count, :]
    return total

def vertical(padded, kernel, count):
    total = jnp.zeros((count, padded.shape[1], padded.shape[2]), jnp.float32)
    for offset in range(kernel.shape[0]):
        total = total + kernel[offset] * padded[offset:offset + count, :, :]
    return total

def tap_sums(left, padded, reduce_dimension):
    length = left.shape[reduce_dimension]
    wide = left.astype(jnp.float32)
    rows_out = []
    for offset in range(padded.shape[reduce_dimension] - length + 1):
        window = lax.slice_in_dim(padded, offset, offset + length, axis=reduce_dimension)
        rows_out.append(lax.optimization_barrier(jnp.sum(wide * window.astype(jnp.float32), axis=(0, 1))))
    return jnp.stack(rows_out)

def pointwise(features, mixed, teacher, norm_gain_vector, weight_in, weight_out):
    shape = features.shape
    chans = shape[-1]
    summed_in = features.astype(jnp.float32).reshape(-1, chans) + mixed.reshape(-1, chans)
    centre = lax.optimization_barrier(jnp.mean(summed_in, axis=-1, keepdims=True))
    mean_removed = summed_in - centre
    spread = lax.optimization_barrier(jnp.mean(mean_removed * mean_removed, axis=-1, keepdims=True))
    inverse_deviation = lax.rsqrt(spread + 1e-06)
    standardized_input = mean_removed * inverse_deviation
    normalized_input = (standardized_input * norm_gain_vector).astype(jnp.bfloat16)
    pre = jnp.dot(normalized_input, weight_in, preferred_element_type=jnp.float32)
    cdf = 0.5 * (1.0 + lax.erf(pre * root_half))
    activ = (pre * cdf).astype(jnp.bfloat16)
    total = summed_in + jnp.dot(activ, weight_out, preferred_element_type=jnp.float32)
    student = total.astype(jnp.bfloat16)
    feature_residual = (total - teacher.astype(jnp.float32).reshape(-1, chans)).astype(jnp.bfloat16)
    grad_out = lax.dot_general(activ, feature_residual, (((0,), (0,)), ((), ())), preferred_element_type=jnp.float32)
    back_act = lax.dot_general(feature_residual, weight_out, (((1,), (1,)), ((), ())), preferred_element_type=jnp.float32)
    slope = cdf + pre * jnp.exp(-0.5 * pre * pre) * inv_root_two_pi
    back_pre = (back_act * slope).astype(jnp.bfloat16)
    grad_in = lax.dot_general(normalized_input, back_pre, (((0,), (0,)), ((), ())), preferred_element_type=jnp.float32)
    norm_backward = lax.dot_general(back_pre, weight_in, (((1,), (1,)), ((), ())), preferred_element_type=jnp.float32)
    gain_gradient = lax.optimization_barrier(jnp.sum(norm_backward * standardized_input, axis=0))
    gain_scaled = norm_backward * norm_gain_vector
    backward_total = feature_residual.astype(jnp.float32) + inverse_deviation * (gain_scaled - lax.optimization_barrier(jnp.mean(gain_scaled, axis=-1, keepdims=True)) - standardized_input * lax.optimization_barrier(jnp.mean(gain_scaled * standardized_input, axis=-1, keepdims=True)))
    backward_total = backward_total.astype(jnp.bfloat16)
    return (student.reshape(shape), backward_total.reshape(shape), grad_in, grad_out, gain_gradient)

def reference(features, teacher, kernel_horiz, kernel_vert, norm_gain_vector, weight_in, weight_out):
    padded_x = jnp.pad(features, ((0, 0), (HALF, HALF), (0, 0)))
    first = horizontal(padded_x, kernel_horiz, WIDTH).astype(jnp.bfloat16)
    padded_first = jnp.pad(first, ((HALF, HALF), (0, 0), (0, 0)))
    second = vertical(padded_first, kernel_vert, HEIGHT)
    blocks = HEIGHT // ROWS_DEV

    def one_block(items):
        return pointwise(items[0], items[1], items[2], norm_gain_vector, weight_in, weight_out)
    stacked = lax.map(one_block, (features.reshape(blocks, ROWS_DEV, WIDTH, C), second.reshape(blocks, ROWS_DEV, WIDTH, C), teacher.reshape(blocks, ROWS_DEV, WIDTH, C)))
    student = stacked[0].reshape(HEIGHT, WIDTH, C)
    backward_total = stacked[1].reshape(HEIGHT, WIDTH, C)
    grad_in = lax.optimization_barrier(jnp.sum(stacked[2], axis=0))
    grad_out = lax.optimization_barrier(jnp.sum(stacked[3], axis=0))
    gain_gradient = lax.optimization_barrier(jnp.sum(stacked[4], axis=0))
    grad_vert = tap_sums(backward_total, padded_first, 0)
    padded_back = jnp.pad(backward_total, ((HALF, HALF), (0, 0), (0, 0)))
    back_first = vertical(padded_back, kernel_vert[::-1], HEIGHT).astype(jnp.bfloat16)
    grad_horiz = tap_sums(back_first, padded_x, 1)
    padded_bf = jnp.pad(back_first, ((0, 0), (HALF, HALF), (0, 0)))
    grad_features = (backward_total.astype(jnp.float32) + horizontal(padded_bf, kernel_horiz[::-1], WIDTH)).astype(jnp.bfloat16)
    factor = 1.0 / jnp.sqrt(jnp.float32(HEIGHT * WIDTH))
    return (student, grad_features, grad_in * factor, grad_out * factor, grad_horiz * factor, grad_vert * factor, gain_gradient * factor)
```

```python
import jax
import jax.numpy as jnp
from jax import lax
from jax.sharding import PartitionSpec as P

root_half = 0.7071067811865476
inv_root_two_pi = 0.3989422804014327


def extended(x, sides, width):
    for axis, dim in sides:
        size, length = (lax.axis_size(axis), x.shape[dim])
        up = [(i, (i + 1) % size) for i in range(size - 1)]
        down = [(j, i) for i, j in up]
        last = lax.slice_in_dim(x, length - width, length, axis=dim)
        initial = lax.slice_in_dim(x, 0, width, axis=dim)
        before = lax.ppermute(last, axis, up)
        after = lax.ppermute(initial, axis, down)
        x = jnp.concatenate([before, x, after], axis=dim)
    return x


def horizontal(padded, kernel, count):
    total = jnp.zeros((padded.shape[0], count, padded.shape[2]), jnp.float32)
    for offset in range(kernel.shape[0]):
        total = total + kernel[offset] * padded[:, offset : offset + count, :]
    return total


def vertical(padded, kernel, count):
    total = jnp.zeros((count, padded.shape[1], padded.shape[2]), jnp.float32)
    for offset in range(kernel.shape[0]):
        total = total + kernel[offset] * padded[offset : offset + count, :, :]
    return total


def tap_sums(left, padded, reduce_dimension):
    length = left.shape[reduce_dimension]
    wide = left.astype(jnp.float32)
    rows_out = []
    for offset in range(padded.shape[reduce_dimension] - length + 1):
        window = lax.slice_in_dim(padded, offset, offset + length, axis=reduce_dimension)
        rows_out.append(jnp.sum(wide * window.astype(jnp.float32), axis=(0, 1)))
    return jnp.stack(rows_out)


def tree_sum(x, axes):
    for axis in axes:
        size = lax.axis_size(axis)
        if size & (size - 1):
            x = lax.psum(x, axis)
            continue
        step = 1
        while step < size:
            x = x + lax.ppermute(x, axis, [(i, i ^ step) for i in range(size)])
            step *= 2
    return x


def pointwise(features, mixed, teacher, norm_gain_vector, weight_in, weight_out):
    shape = features.shape
    chans = shape[-1]
    summed_in = features.astype(jnp.float32).reshape(-1, chans) + mixed.reshape(-1, chans)
    centre = jnp.mean(summed_in, axis=-1, keepdims=True)
    mean_removed = summed_in - centre
    spread = jnp.mean(mean_removed * mean_removed, axis=-1, keepdims=True)
    inverse_deviation = lax.rsqrt(spread + 1e-06)
    standardized_input = mean_removed * inverse_deviation
    normalized_input = (standardized_input * norm_gain_vector).astype(jnp.bfloat16)
    pre = jnp.dot(normalized_input, weight_in, preferred_element_type=jnp.float32)
    cdf = 0.5 * (1.0 + lax.erf(pre * root_half))
    activ = (pre * cdf).astype(jnp.bfloat16)
    total = summed_in + jnp.dot(activ, weight_out, preferred_element_type=jnp.float32)
    student = total.astype(jnp.bfloat16)
    feature_residual = (total - teacher.astype(jnp.float32).reshape(-1, chans)).astype(jnp.bfloat16)
    grad_out = lax.dot_general(
        activ, feature_residual, (((0,), (0,)), ((), ())), preferred_element_type=jnp.float32
    )
    back_act = lax.dot_general(
        feature_residual, weight_out, (((1,), (1,)), ((), ())), preferred_element_type=jnp.float32
    )
    slope = cdf + pre * jnp.exp(-0.5 * pre * pre) * inv_root_two_pi
    back_pre = (back_act * slope).astype(jnp.bfloat16)
    grad_in = lax.dot_general(
        normalized_input, back_pre, (((0,), (0,)), ((), ())), preferred_element_type=jnp.float32
    )
    norm_backward = lax.dot_general(
        back_pre, weight_in, (((1,), (1,)), ((), ())), preferred_element_type=jnp.float32
    )
    gain_gradient = jnp.sum(norm_backward * standardized_input, axis=0)
    gain_scaled = norm_backward * norm_gain_vector
    backward_total = feature_residual.astype(jnp.float32) + inverse_deviation * (
        gain_scaled
        - jnp.mean(gain_scaled, axis=-1, keepdims=True)
        - standardized_input * jnp.mean(gain_scaled * standardized_input, axis=-1, keepdims=True)
    )
    backward_total = backward_total.astype(jnp.bfloat16)
    return (student.reshape(shape), backward_total.reshape(shape), grad_in, grad_out, gain_gradient)


def on_device(
    features, teacher, kernel_horiz, kernel_vert, norm_gain_vector, weight_in, weight_out
):
    rows_here = features.shape[0]
    cols_here = features.shape[1]
    margin = (kernel_horiz.shape[0] - 1) // 2
    padded_x = extended(features, (("col", 1),), margin)
    first = horizontal(padded_x, kernel_horiz, cols_here).astype(jnp.bfloat16)
    padded_first = extended(first, (("row", 0),), margin)
    second = vertical(padded_first, kernel_vert, rows_here)
    student, backward_total, grad_in, grad_out, gain_gradient = pointwise(
        features, second, teacher, norm_gain_vector, weight_in, weight_out
    )
    grad_vert = tap_sums(backward_total, padded_first, 0)
    padded_back = extended(backward_total, (("row", 0),), margin)
    back_first = vertical(padded_back, kernel_vert[::-1], rows_here).astype(jnp.bfloat16)
    padded_bf = extended(back_first, (("col", 1),), margin)
    grad_horiz = tap_sums(back_first, padded_x, 1)
    grad_features = (
        backward_total.astype(jnp.float32) + horizontal(padded_bf, kernel_horiz[::-1], cols_here)
    ).astype(jnp.bfloat16)
    big = lax.psum((grad_in, grad_out), ("row", "col"))
    taps = tree_sum(
        jnp.concatenate([grad_horiz, grad_vert, gain_gradient[None]], axis=0), ("col", "row")
    )
    count = grad_horiz.shape[0]
    totals = (big[0], big[1], taps[:count], taps[count : 2 * count], taps[2 * count])
    cells = rows_here * lax.axis_size("row") * cols_here * lax.axis_size("col")
    factor = 1.0 / jnp.sqrt(jnp.float32(cells))
    return (
        student,
        grad_features,
        totals[0] * factor,
        totals[1] * factor,
        totals[2] * factor,
        totals[3] * factor,
        totals[4] * factor,
    )


def solution(mesh):
    return jax.shard_map(
        on_device,
        mesh=mesh,
        in_specs=(
            P(("slab", "row"), "col", None),
            P(("slab", "row"), "col", None),
            P(),
            P(),
            P(),
            P(),
            P(),
        ),
        out_specs=(
            P(("slab", "row"), "col", None),
            P(("slab", "row"), "col", None),
            P("slab", None),
            P("slab", None),
            P("slab", None),
            P("slab", None),
            P("slab"),
        ),
        check_vma=False,
    )
```

```python
import jax
import jax.numpy as jnp
from jax import lax
from jax.sharding import PartitionSpec as P

root_half = 0.7071067811865476
inv_root_two_pi = 0.3989422804014327


def extended(x, sides, width):
    for axis, dim in sides:
        size, length = (lax.axis_size(axis), x.shape[dim])
        up = [(i, (i + 1) % size) for i in range(size - 1)]
        down = [(j, i) for i, j in up]
        last = lax.slice_in_dim(x, length - width, length, axis=dim)
        initial = lax.slice_in_dim(x, 0, width, axis=dim)
        before = lax.ppermute(last, axis, up)
        after = lax.ppermute(initial, axis, down)
        x = jnp.concatenate([before, x, after], axis=dim)
    return x


def horizontal(padded, kernel, count):
    total = jnp.zeros((padded.shape[0], count, padded.shape[2]), jnp.float32)
    for offset in range(kernel.shape[0]):
        total = total + kernel[offset] * padded[:, offset : offset + count, :]
    return total


def vertical(padded, kernel, count):
    total = jnp.zeros((count, padded.shape[1], padded.shape[2]), jnp.float32)
    for offset in range(kernel.shape[0]):
        total = total + kernel[offset] * padded[offset : offset + count, :, :]
    return total


def tap_sums(left, padded, reduce_dimension):
    length = left.shape[reduce_dimension]
    wide = left.astype(jnp.float32)
    rows_out = []
    for offset in range(padded.shape[reduce_dimension] - length + 1):
        window = lax.slice_in_dim(padded, offset, offset + length, axis=reduce_dimension)
        rows_out.append(jnp.sum(wide * window.astype(jnp.float32), axis=(0, 1)))
    return jnp.stack(rows_out)


def tree_sum(x, axes):
    for axis in axes:
        size = lax.axis_size(axis)
        if size & (size - 1):
            x = lax.psum(x, axis)
            continue
        step = 1
        while step < size:
            x = x + lax.ppermute(x, axis, [(i, i ^ step) for i in range(size)])
            step *= 2
    return x


def pointwise(features, mixed, teacher, norm_gain_vector, weight_in, weight_out):
    shape = features.shape
    chans = shape[-1]
    summed_in = features.astype(jnp.float32).reshape(-1, chans) + mixed.reshape(-1, chans)
    centre = jnp.mean(summed_in, axis=-1, keepdims=True)
    mean_removed = summed_in - centre
    spread = jnp.mean(mean_removed * mean_removed, axis=-1, keepdims=True)
    inverse_deviation = lax.rsqrt(spread + 1e-06)
    standardized_input = mean_removed * inverse_deviation
    normalized_input = (standardized_input * norm_gain_vector).astype(jnp.bfloat16)
    pre = jnp.dot(normalized_input, weight_in, preferred_element_type=jnp.float32)
    cdf = 0.5 * (1.0 + lax.erf(pre * root_half))
    activ = (pre * cdf).astype(jnp.bfloat16)
    total = summed_in + jnp.dot(activ, weight_out, preferred_element_type=jnp.float32)
    student = total.astype(jnp.bfloat16)
    feature_residual = (total - teacher.astype(jnp.float32).reshape(-1, chans)).astype(jnp.bfloat16)
    grad_out = lax.dot_general(
        activ, feature_residual, (((0,), (0,)), ((), ())), preferred_element_type=jnp.float32
    )
    back_act = lax.dot_general(
        feature_residual, weight_out, (((1,), (1,)), ((), ())), preferred_element_type=jnp.float32
    )
    slope = cdf + pre * jnp.exp(-0.5 * pre * pre) * inv_root_two_pi
    back_pre = (back_act * slope).astype(jnp.bfloat16)
    grad_in = lax.dot_general(
        normalized_input, back_pre, (((0,), (0,)), ((), ())), preferred_element_type=jnp.float32
    )
    norm_backward = lax.dot_general(
        back_pre, weight_in, (((1,), (1,)), ((), ())), preferred_element_type=jnp.float32
    )
    gain_gradient = jnp.sum(norm_backward * standardized_input, axis=0)
    gain_scaled = norm_backward * norm_gain_vector
    backward_total = feature_residual.astype(jnp.float32) + inverse_deviation * (
        gain_scaled
        - jnp.mean(gain_scaled, axis=-1, keepdims=True)
        - standardized_input * jnp.mean(gain_scaled * standardized_input, axis=-1, keepdims=True)
    )
    backward_total = backward_total.astype(jnp.bfloat16)
    return (student.reshape(shape), backward_total.reshape(shape), grad_in, grad_out, gain_gradient)


def on_device(
    features, teacher, kernel_horiz, kernel_vert, norm_gain_vector, weight_in, weight_out
):
    rows_here = features.shape[0]
    cols_here = features.shape[1]
    margin = (kernel_horiz.shape[0] - 1) // 2
    parts = 4 if cols_here % 32 == 0 else 1
    width = cols_here // parts
    padded_x = extended(features, (("col", 1),), margin)
    pieces = []
    for k in range(parts):
        low = k * width
        first = horizontal(
            padded_x[:, low : low + width + 2 * margin], kernel_horiz, width
        ).astype(jnp.bfloat16)
        padded_first = extended(first, (("row", 0),), margin)
        second = vertical(padded_first, kernel_vert, rows_here)
        student, backward_total, grad_in, grad_out, gain_gradient = pointwise(
            features[:, low : low + width],
            second,
            teacher[:, low : low + width],
            norm_gain_vector,
            weight_in,
            weight_out,
        )
        grad_vert = tap_sums(backward_total, padded_first, 0)
        padded_back = extended(backward_total, (("row", 0),), margin)
        back_first = vertical(padded_back, kernel_vert[::-1], rows_here).astype(jnp.bfloat16)
        pieces.append(
            (student, backward_total, back_first, grad_in, grad_out, gain_gradient, grad_vert)
        )
    student = jnp.concatenate([p[0] for p in pieces], axis=1)
    backward_total = jnp.concatenate([p[1] for p in pieces], axis=1)
    back_first = jnp.concatenate([p[2] for p in pieces], axis=1)
    grad_in, grad_out, gain_gradient, grad_vert = (
        sum(p[i] for p in pieces[1:]) + pieces[0][i] for i in range(3, 7)
    )
    big = lax.psum((grad_in, grad_out), ("row", "col"))
    padded_bf = extended(back_first, (("col", 1),), margin)
    grad_horiz = tap_sums(back_first, padded_x, 1)
    grad_features = (
        backward_total.astype(jnp.float32) + horizontal(padded_bf, kernel_horiz[::-1], cols_here)
    ).astype(jnp.bfloat16)
    taps = tree_sum(
        jnp.concatenate([grad_horiz, grad_vert, gain_gradient[None]], axis=0), ("col", "row")
    )
    count = grad_horiz.shape[0]
    totals = (big[0], big[1], taps[:count], taps[count : 2 * count], taps[2 * count])
    cells = rows_here * lax.axis_size("row") * cols_here * lax.axis_size("col")
    factor = 1.0 / jnp.sqrt(jnp.float32(cells))
    return (
        student,
        grad_features,
        totals[0] * factor,
        totals[1] * factor,
        totals[2] * factor,
        totals[3] * factor,
        totals[4] * factor,
    )


def solution(mesh):
    return jax.shard_map(
        on_device,
        mesh=mesh,
        in_specs=(
            P(("slab", "row"), "col", None),
            P(("slab", "row"), "col", None),
            P(),
            P(),
            P(),
            P(),
            P(),
        ),
        out_specs=(
            P(("slab", "row"), "col", None),
            P(("slab", "row"), "col", None),
            P("slab", None),
            P("slab", None),
            P("slab", None),
            P("slab", None),
            P("slab"),
        ),
        check_vma=False,
    )
```

```python
import jax
import jax.numpy as jnp
from jax import lax
from jax.sharding import PartitionSpec as P

root_half = 0.7071067811865476
inv_root_two_pi = 0.3989422804014327


def extended(x, sides, width):
    for axis, dim in sides:
        size, length = (lax.axis_size(axis), x.shape[dim])
        up = [(i, (i + 1) % size) for i in range(size - 1)]
        down = [(j, i) for i, j in up]
        last = lax.slice_in_dim(x, length - width, length, axis=dim)
        initial = lax.slice_in_dim(x, 0, width, axis=dim)
        before = lax.ppermute(last, axis, up)
        after = lax.ppermute(initial, axis, down)
        x = jnp.concatenate([before, x, after], axis=dim)
    return x


def horizontal(padded, kernel, count):
    total = jnp.zeros((padded.shape[0], count, padded.shape[2]), jnp.float32)
    for offset in range(kernel.shape[0]):
        total = total + kernel[offset] * padded[:, offset : offset + count, :]
    return total


def vertical(padded, kernel, count):
    total = jnp.zeros((count, padded.shape[1], padded.shape[2]), jnp.float32)
    for offset in range(kernel.shape[0]):
        total = total + kernel[offset] * padded[offset : offset + count, :, :]
    return total


def tap_sums(left, padded, reduce_dimension):
    length = left.shape[reduce_dimension]
    wide = left.astype(jnp.float32)
    rows_out = []
    for offset in range(padded.shape[reduce_dimension] - length + 1):
        window = lax.slice_in_dim(padded, offset, offset + length, axis=reduce_dimension)
        rows_out.append(jnp.sum(wide * window.astype(jnp.float32), axis=(0, 1)))
    return jnp.stack(rows_out)


def tree_sum(x, axes):
    for axis in axes:
        size = lax.axis_size(axis)
        if size & (size - 1):
            x = lax.psum(x, axis)
            continue
        step = 1
        while step < size:
            x = x + lax.ppermute(x, axis, [(i, i ^ step) for i in range(size)])
            step *= 2
    return x


def pointwise(features, mixed, teacher, norm_gain_vector, weight_in, weight_out):
    shape = features.shape
    chans = shape[-1]
    summed_in = features.astype(jnp.float32).reshape(-1, chans) + mixed.reshape(-1, chans)
    centre = jnp.mean(summed_in, axis=-1, keepdims=True)
    mean_removed = summed_in - centre
    spread = jnp.mean(mean_removed * mean_removed, axis=-1, keepdims=True)
    inverse_deviation = lax.rsqrt(spread + 1e-06)
    standardized_input = mean_removed * inverse_deviation
    normalized_input = (standardized_input * norm_gain_vector).astype(jnp.bfloat16)
    pre = jnp.dot(normalized_input, weight_in, preferred_element_type=jnp.float32)
    cdf = 0.5 * (1.0 + lax.erf(pre * root_half))
    activ = (pre * cdf).astype(jnp.bfloat16)
    total = summed_in + jnp.dot(activ, weight_out, preferred_element_type=jnp.float32)
    student = total.astype(jnp.bfloat16)
    feature_residual = (total - teacher.astype(jnp.float32).reshape(-1, chans)).astype(jnp.bfloat16)
    grad_out = lax.dot_general(
        activ, feature_residual, (((0,), (0,)), ((), ())), preferred_element_type=jnp.float32
    )
    back_act = lax.dot_general(
        feature_residual, weight_out, (((1,), (1,)), ((), ())), preferred_element_type=jnp.float32
    )
    slope = cdf + pre * jnp.exp(-0.5 * pre * pre) * inv_root_two_pi
    back_pre = (back_act * slope).astype(jnp.bfloat16)
    grad_in = lax.dot_general(
        normalized_input, back_pre, (((0,), (0,)), ((), ())), preferred_element_type=jnp.float32
    )
    norm_backward = lax.dot_general(
        back_pre, weight_in, (((1,), (1,)), ((), ())), preferred_element_type=jnp.float32
    )
    gain_gradient = jnp.sum(norm_backward * standardized_input, axis=0)
    gain_scaled = norm_backward * norm_gain_vector
    backward_total = feature_residual.astype(jnp.float32) + inverse_deviation * (
        gain_scaled
        - jnp.mean(gain_scaled, axis=-1, keepdims=True)
        - standardized_input * jnp.mean(gain_scaled * standardized_input, axis=-1, keepdims=True)
    )
    backward_total = backward_total.astype(jnp.bfloat16)
    return (student.reshape(shape), backward_total.reshape(shape), grad_in, grad_out, gain_gradient)


def on_device(
    features, teacher, kernel_horiz, kernel_vert, norm_gain_vector, weight_in, weight_out
):
    rows_here = features.shape[0]
    cols_here = features.shape[1]
    margin = (kernel_horiz.shape[0] - 1) // 2
    parts = 4 if cols_here % 32 == 0 else 1
    width = cols_here // parts
    padded_x = extended(features, (("col", 1),), margin)
    firsts, seconds = [], []
    for k in range(parts):
        low = k * width
        first = horizontal(
            padded_x[:, low : low + width + 2 * margin], kernel_horiz, width
        ).astype(jnp.bfloat16)
        padded_first = extended(first, (("row", 0),), margin)
        firsts.append(padded_first)
        seconds.append(vertical(padded_first, kernel_vert, rows_here))
    padded_first = jnp.concatenate(firsts, axis=1)
    second = jnp.concatenate(seconds, axis=1)
    student, backward_total, grad_in, grad_out, gain_gradient = pointwise(
        features, second, teacher, norm_gain_vector, weight_in, weight_out
    )
    big = lax.psum((grad_in, grad_out), ("row", "col"))
    grad_vert = tap_sums(backward_total, padded_first, 0)
    padded_back = extended(backward_total, (("row", 0),), margin)
    back_first = vertical(padded_back, kernel_vert[::-1], rows_here).astype(jnp.bfloat16)
    padded_bf = extended(back_first, (("col", 1),), margin)
    grad_horiz = tap_sums(back_first, padded_x, 1)
    grad_features = (
        backward_total.astype(jnp.float32) + horizontal(padded_bf, kernel_horiz[::-1], cols_here)
    ).astype(jnp.bfloat16)
    taps = tree_sum(
        jnp.concatenate([grad_horiz, grad_vert, gain_gradient[None]], axis=0), ("col", "row")
    )
    count = grad_horiz.shape[0]
    totals = (big[0], big[1], taps[:count], taps[count : 2 * count], taps[2 * count])
    cells = rows_here * lax.axis_size("row") * cols_here * lax.axis_size("col")
    factor = 1.0 / jnp.sqrt(jnp.float32(cells))
    return (
        student,
        grad_features,
        totals[0] * factor,
        totals[1] * factor,
        totals[2] * factor,
        totals[3] * factor,
        totals[4] * factor,
    )


def solution(mesh):
    return jax.shard_map(
        on_device,
        mesh=mesh,
        in_specs=(
            P(("slab", "row"), "col", None),
            P(("slab", "row"), "col", None),
            P(),
            P(),
            P(),
            P(),
            P(),
        ),
        out_specs=(
            P(("slab", "row"), "col", None),
            P(("slab", "row"), "col", None),
            P("slab", None),
            P("slab", None),
            P("slab", None),
            P("slab", None),
            P("slab"),
        ),
        check_vma=False,
    )
```

```python
import jax
import jax.numpy as jnp
from jax import lax
from jax.sharding import PartitionSpec as P

root_half = 0.7071067811865476
inv_root_two_pi = 0.3989422804014327


def extended(x, sides, width):
    for axis, dim in sides:
        size, length = (lax.axis_size(axis), x.shape[dim])
        up = [(i, (i + 1) % size) for i in range(size - 1)]
        down = [(j, i) for i, j in up]
        last = lax.slice_in_dim(x, length - width, length, axis=dim)
        initial = lax.slice_in_dim(x, 0, width, axis=dim)
        before = lax.ppermute(last, axis, up)
        after = lax.ppermute(initial, axis, down)
        x = jnp.concatenate([before, x, after], axis=dim)
    return x


def horizontal(padded, kernel, count):
    total = jnp.zeros((padded.shape[0], count, padded.shape[2]), jnp.float32)
    for offset in range(kernel.shape[0]):
        total = total + kernel[offset] * padded[:, offset : offset + count, :]
    return total


def vertical(padded, kernel, count):
    total = jnp.zeros((count, padded.shape[1], padded.shape[2]), jnp.float32)
    for offset in range(kernel.shape[0]):
        total = total + kernel[offset] * padded[offset : offset + count, :, :]
    return total


def tap_sums(left, padded, reduce_dimension):
    length = left.shape[reduce_dimension]
    wide = left.astype(jnp.float32)
    rows_out = []
    for offset in range(padded.shape[reduce_dimension] - length + 1):
        window = lax.slice_in_dim(padded, offset, offset + length, axis=reduce_dimension)
        rows_out.append(jnp.sum(wide * window.astype(jnp.float32), axis=(0, 1)))
    return jnp.stack(rows_out)


def tree_sum(x, axes):
    for axis in axes:
        size = lax.axis_size(axis)
        if size & (size - 1):
            x = lax.psum(x, axis)
            continue
        step = 1
        while step < size:
            x = x + lax.ppermute(x, axis, [(i, i ^ step) for i in range(size)])
            step *= 2
    return x


def pointwise(features, mixed, teacher, norm_gain_vector, weight_in, weight_out):
    shape = features.shape
    chans = shape[-1]
    summed_in = features.astype(jnp.float32).reshape(-1, chans) + mixed.reshape(-1, chans)
    centre = jnp.mean(summed_in, axis=-1, keepdims=True)
    mean_removed = summed_in - centre
    spread = jnp.mean(mean_removed * mean_removed, axis=-1, keepdims=True)
    inverse_deviation = lax.rsqrt(spread + 1e-06)
    standardized_input = mean_removed * inverse_deviation
    normalized_input = (standardized_input * norm_gain_vector).astype(jnp.bfloat16)
    pre = jnp.dot(normalized_input, weight_in, preferred_element_type=jnp.float32)
    cdf = 0.5 * (1.0 + lax.erf(pre * root_half))
    activ = (pre * cdf).astype(jnp.bfloat16)
    total = summed_in + jnp.dot(activ, weight_out, preferred_element_type=jnp.float32)
    student = total.astype(jnp.bfloat16)
    feature_residual = (total - teacher.astype(jnp.float32).reshape(-1, chans)).astype(jnp.bfloat16)
    grad_out = lax.dot_general(
        activ, feature_residual, (((0,), (0,)), ((), ())), preferred_element_type=jnp.float32
    )
    back_act = lax.dot_general(
        feature_residual, weight_out, (((1,), (1,)), ((), ())), preferred_element_type=jnp.float32
    )
    slope = cdf + pre * jnp.exp(-0.5 * pre * pre) * inv_root_two_pi
    back_pre = (back_act * slope).astype(jnp.bfloat16)
    grad_in = lax.dot_general(
        normalized_input, back_pre, (((0,), (0,)), ((), ())), preferred_element_type=jnp.float32
    )
    norm_backward = lax.dot_general(
        back_pre, weight_in, (((1,), (1,)), ((), ())), preferred_element_type=jnp.float32
    )
    gain_gradient = jnp.sum(norm_backward * standardized_input, axis=0)
    gain_scaled = norm_backward * norm_gain_vector
    backward_total = feature_residual.astype(jnp.float32) + inverse_deviation * (
        gain_scaled
        - jnp.mean(gain_scaled, axis=-1, keepdims=True)
        - standardized_input * jnp.mean(gain_scaled * standardized_input, axis=-1, keepdims=True)
    )
    backward_total = backward_total.astype(jnp.bfloat16)
    return (student.reshape(shape), backward_total.reshape(shape), grad_in, grad_out, gain_gradient)


def on_device(
    features, teacher, kernel_horiz, kernel_vert, norm_gain_vector, weight_in, weight_out
):
    rows_here = features.shape[0]
    cols_here = features.shape[1]
    margin = (kernel_horiz.shape[0] - 1) // 2
    parts = 4 if cols_here % 32 == 0 else 1
    width = cols_here // parts
    padded_x = extended(features, (("col", 1),), margin)
    firsts, seconds = [], []
    for k in range(parts):
        low = k * width
        first = horizontal(
            padded_x[:, low : low + width + 2 * margin], kernel_horiz, width
        ).astype(jnp.bfloat16)
        padded_first = extended(first, (("row", 0),), margin)
        firsts.append(padded_first)
        seconds.append(vertical(padded_first, kernel_vert, rows_here))
    second = jnp.concatenate(seconds, axis=1)
    student, backward_total, grad_in, grad_out, gain_gradient = pointwise(
        features, second, teacher, norm_gain_vector, weight_in, weight_out
    )
    big = lax.psum((grad_in, grad_out), ("row", "col"))
    backs, grad_vert = [], 0.0
    for k in range(parts):
        piece = backward_total[:, k * width : (k + 1) * width]
        padded_back = extended(piece, (("row", 0),), margin)
        backs.append(vertical(padded_back, kernel_vert[::-1], rows_here).astype(jnp.bfloat16))
        grad_vert = grad_vert + tap_sums(piece, firsts[k], 0)
    back_first = jnp.concatenate(backs, axis=1)
    padded_bf = extended(back_first, (("col", 1),), margin)
    grad_horiz = tap_sums(back_first, padded_x, 1)
    grad_features = (
        backward_total.astype(jnp.float32) + horizontal(padded_bf, kernel_horiz[::-1], cols_here)
    ).astype(jnp.bfloat16)
    taps = tree_sum(
        jnp.concatenate([grad_horiz, grad_vert, gain_gradient[None]], axis=0), ("col", "row")
    )
    count = grad_horiz.shape[0]
    totals = (big[0], big[1], taps[:count], taps[count : 2 * count], taps[2 * count])
    cells = rows_here * lax.axis_size("row") * cols_here * lax.axis_size("col")
    factor = 1.0 / jnp.sqrt(jnp.float32(cells))
    return (
        student,
        grad_features,
        totals[0] * factor,
        totals[1] * factor,
        totals[2] * factor,
        totals[3] * factor,
        totals[4] * factor,
    )


def solution(mesh):
    return jax.shard_map(
        on_device,
        mesh=mesh,
        in_specs=(
            P(("slab", "row"), "col", None),
            P(("slab", "row"), "col", None),
            P(),
            P(),
            P(),
            P(),
            P(),
        ),
        out_specs=(
            P(("slab", "row"), "col", None),
            P(("slab", "row"), "col", None),
            P("slab", None),
            P("slab", None),
            P("slab", None),
            P("slab", None),
            P("slab"),
        ),
        check_vma=False,
    )
```

```python
import jax
import jax.numpy as jnp
from jax import lax
from jax.sharding import PartitionSpec as P

root_half = 0.7071067811865476
inv_root_two_pi = 0.3989422804014327


def extended(x, sides, width):
    for axis, dim in sides:
        size, length = (lax.axis_size(axis), x.shape[dim])
        up = [(i, (i + 1) % size) for i in range(size - 1)]
        down = [(j, i) for i, j in up]
        last = lax.slice_in_dim(x, length - width, length, axis=dim)
        initial = lax.slice_in_dim(x, 0, width, axis=dim)
        before = lax.ppermute(last, axis, up)
        after = lax.ppermute(initial, axis, down)
        x = jnp.concatenate([before, x, after], axis=dim)
    return x


def horizontal(padded, kernel, count):
    total = jnp.zeros((padded.shape[0], count, padded.shape[2]), jnp.float32)
    for offset in range(kernel.shape[0]):
        total = total + kernel[offset] * padded[:, offset : offset + count, :]
    return total


def vertical(padded, kernel, count):
    total = jnp.zeros((count, padded.shape[1], padded.shape[2]), jnp.float32)
    for offset in range(kernel.shape[0]):
        total = total + kernel[offset] * padded[offset : offset + count, :, :]
    return total


def tap_sums(left, padded, reduce_dimension):
    length = left.shape[reduce_dimension]
    wide = left.astype(jnp.float32)
    rows_out = []
    for offset in range(padded.shape[reduce_dimension] - length + 1):
        window = lax.slice_in_dim(padded, offset, offset + length, axis=reduce_dimension)
        rows_out.append(jnp.sum(wide * window.astype(jnp.float32), axis=(0, 1)))
    return jnp.stack(rows_out)


def tree_sum(x, axes):
    for axis in axes:
        size = lax.axis_size(axis)
        if size & (size - 1):
            x = lax.psum(x, axis)
            continue
        step = 1
        while step < size:
            x = x + lax.ppermute(x, axis, [(i, i ^ step) for i in range(size)])
            step *= 2
    return x


def staged_sum(values):
    if any(v.shape[0] % lax.axis_size("col") for v in values):
        return lax.psum(values, ("row", "col"))
    halves = lax.psum_scatter(values, "col", scatter_dimension=0, tiled=True)
    halves = lax.psum(halves, "row")
    return lax.all_gather(halves, "col", axis=0, tiled=True)


def pointwise(features, mixed, teacher, norm_gain_vector, weight_in, weight_out):
    shape = features.shape
    chans = shape[-1]
    summed_in = features.astype(jnp.float32).reshape(-1, chans) + mixed.reshape(-1, chans)
    centre = jnp.mean(summed_in, axis=-1, keepdims=True)
    mean_removed = summed_in - centre
    spread = jnp.mean(mean_removed * mean_removed, axis=-1, keepdims=True)
    inverse_deviation = lax.rsqrt(spread + 1e-06)
    standardized_input = mean_removed * inverse_deviation
    normalized_input = (standardized_input * norm_gain_vector).astype(jnp.bfloat16)
    pre = jnp.dot(normalized_input, weight_in, preferred_element_type=jnp.float32)
    cdf = 0.5 * (1.0 + lax.erf(pre * root_half))
    activ = (pre * cdf).astype(jnp.bfloat16)
    total = summed_in + jnp.dot(activ, weight_out, preferred_element_type=jnp.float32)
    student = total.astype(jnp.bfloat16)
    feature_residual = (total - teacher.astype(jnp.float32).reshape(-1, chans)).astype(jnp.bfloat16)
    grad_out = lax.dot_general(
        activ, feature_residual, (((0,), (0,)), ((), ())), preferred_element_type=jnp.float32
    )
    back_act = lax.dot_general(
        feature_residual, weight_out, (((1,), (1,)), ((), ())), preferred_element_type=jnp.float32
    )
    slope = cdf + pre * jnp.exp(-0.5 * pre * pre) * inv_root_two_pi
    back_pre = (back_act * slope).astype(jnp.bfloat16)
    grad_in = lax.dot_general(
        normalized_input, back_pre, (((0,), (0,)), ((), ())), preferred_element_type=jnp.float32
    )
    norm_backward = lax.dot_general(
        back_pre, weight_in, (((1,), (1,)), ((), ())), preferred_element_type=jnp.float32
    )
    gain_gradient = jnp.sum(norm_backward * standardized_input, axis=0)
    gain_scaled = norm_backward * norm_gain_vector
    backward_total = feature_residual.astype(jnp.float32) + inverse_deviation * (
        gain_scaled
        - jnp.mean(gain_scaled, axis=-1, keepdims=True)
        - standardized_input * jnp.mean(gain_scaled * standardized_input, axis=-1, keepdims=True)
    )
    backward_total = backward_total.astype(jnp.bfloat16)
    return (student.reshape(shape), backward_total.reshape(shape), grad_in, grad_out, gain_gradient)


def on_device(
    features, teacher, kernel_horiz, kernel_vert, norm_gain_vector, weight_in, weight_out
):
    rows_here = features.shape[0]
    cols_here = features.shape[1]
    margin = (kernel_horiz.shape[0] - 1) // 2
    parts = 4 if cols_here % 32 == 0 else 1
    width = cols_here // parts
    padded_x = extended(features, (("col", 1),), margin)
    firsts, seconds = [], []
    for k in range(parts):
        low = k * width
        first = horizontal(
            padded_x[:, low : low + width + 2 * margin], kernel_horiz, width
        ).astype(jnp.bfloat16)
        padded_first = extended(first, (("row", 0),), margin)
        firsts.append(padded_first)
        seconds.append(vertical(padded_first, kernel_vert, rows_here))
    second = jnp.concatenate(seconds, axis=1)
    student, backward_total, grad_in, grad_out, gain_gradient = pointwise(
        features, second, teacher, norm_gain_vector, weight_in, weight_out
    )
    big = staged_sum((grad_in, grad_out))
    backs, grad_vert = [], 0.0
    for k in range(parts):
        piece = backward_total[:, k * width : (k + 1) * width]
        padded_back = extended(piece, (("row", 0),), margin)
        backs.append(vertical(padded_back, kernel_vert[::-1], rows_here).astype(jnp.bfloat16))
        grad_vert = grad_vert + tap_sums(piece, firsts[k], 0)
    back_first = jnp.concatenate(backs, axis=1)
    padded_bf = extended(back_first, (("col", 1),), margin)
    grad_horiz = tap_sums(back_first, padded_x, 1)
    grad_features = (
        backward_total.astype(jnp.float32) + horizontal(padded_bf, kernel_horiz[::-1], cols_here)
    ).astype(jnp.bfloat16)
    taps = tree_sum(
        jnp.concatenate([grad_horiz, grad_vert, gain_gradient[None]], axis=0), ("col", "row")
    )
    count = grad_horiz.shape[0]
    totals = (big[0], big[1], taps[:count], taps[count : 2 * count], taps[2 * count])
    cells = rows_here * lax.axis_size("row") * cols_here * lax.axis_size("col")
    factor = 1.0 / jnp.sqrt(jnp.float32(cells))
    return (
        student,
        grad_features,
        totals[0] * factor,
        totals[1] * factor,
        totals[2] * factor,
        totals[3] * factor,
        totals[4] * factor,
    )


def solution(mesh):
    return jax.shard_map(
        on_device,
        mesh=mesh,
        in_specs=(
            P(("slab", "row"), "col", None),
            P(("slab", "row"), "col", None),
            P(),
            P(),
            P(),
            P(),
            P(),
        ),
        out_specs=(
            P(("slab", "row"), "col", None),
            P(("slab", "row"), "col", None),
            P("slab", None),
            P("slab", None),
            P("slab", None),
            P("slab", None),
            P("slab"),
        ),
        check_vma=False,
    )
```

```python
import jax
import jax.numpy as jnp
from jax import lax
from jax.sharding import PartitionSpec as P

root_half = 0.7071067811865476
inv_root_two_pi = 0.3989422804014327


def extended(x, sides, width):
    for axis, dim in sides:
        size, length = (lax.axis_size(axis), x.shape[dim])
        up = [(i, (i + 1) % size) for i in range(size - 1)]
        down = [(j, i) for i, j in up]
        last = lax.slice_in_dim(x, length - width, length, axis=dim)
        initial = lax.slice_in_dim(x, 0, width, axis=dim)
        before = lax.ppermute(last, axis, up)
        after = lax.ppermute(initial, axis, down)
        x = jnp.concatenate([before, x, after], axis=dim)
    return x


def horizontal(padded, kernel, count):
    total = jnp.zeros((padded.shape[0], count, padded.shape[2]), jnp.float32)
    for offset in range(kernel.shape[0]):
        total = total + kernel[offset] * padded[:, offset : offset + count, :]
    return total


def vertical(padded, kernel, count):
    total = jnp.zeros((count, padded.shape[1], padded.shape[2]), jnp.float32)
    for offset in range(kernel.shape[0]):
        total = total + kernel[offset] * padded[offset : offset + count, :, :]
    return total


def tap_sums(left, padded, reduce_dimension):
    length = left.shape[reduce_dimension]
    wide = left.astype(jnp.float32)
    rows_out = []
    for offset in range(padded.shape[reduce_dimension] - length + 1):
        window = lax.slice_in_dim(padded, offset, offset + length, axis=reduce_dimension)
        rows_out.append(jnp.sum(wide * window.astype(jnp.float32), axis=(0, 1)))
    return jnp.stack(rows_out)


def tree_sum(x, axes):
    for axis in axes:
        size = lax.axis_size(axis)
        if size & (size - 1):
            x = lax.psum(x, axis)
            continue
        step = 1
        while step < size:
            x = x + lax.ppermute(x, axis, [(i, i ^ step) for i in range(size)])
            step *= 2
    return x


def pointwise(features, mixed, teacher, norm_gain_vector, weight_in, weight_out):
    shape = features.shape
    chans = shape[-1]
    summed_in = features.astype(jnp.float32).reshape(-1, chans) + mixed.reshape(-1, chans)
    centre = jnp.mean(summed_in, axis=-1, keepdims=True)
    mean_removed = summed_in - centre
    spread = jnp.mean(mean_removed * mean_removed, axis=-1, keepdims=True)
    inverse_deviation = lax.rsqrt(spread + 1e-06)
    standardized_input = mean_removed * inverse_deviation
    normalized_input = (standardized_input * norm_gain_vector).astype(jnp.bfloat16)
    pre = jnp.dot(normalized_input, weight_in, preferred_element_type=jnp.float32)
    cdf = 0.5 * (1.0 + lax.erf(pre * root_half))
    activ = (pre * cdf).astype(jnp.bfloat16)
    total = summed_in + jnp.dot(activ, weight_out, preferred_element_type=jnp.float32)
    student = total.astype(jnp.bfloat16)
    feature_residual = (total - teacher.astype(jnp.float32).reshape(-1, chans)).astype(jnp.bfloat16)
    grad_out = lax.dot_general(
        activ, feature_residual, (((0,), (0,)), ((), ())), preferred_element_type=jnp.float32
    )
    back_act = lax.dot_general(
        feature_residual, weight_out, (((1,), (1,)), ((), ())), preferred_element_type=jnp.float32
    )
    slope = cdf + pre * jnp.exp(-0.5 * pre * pre) * inv_root_two_pi
    back_pre = (back_act * slope).astype(jnp.bfloat16)
    grad_in = lax.dot_general(
        normalized_input, back_pre, (((0,), (0,)), ((), ())), preferred_element_type=jnp.float32
    )
    norm_backward = lax.dot_general(
        back_pre, weight_in, (((1,), (1,)), ((), ())), preferred_element_type=jnp.float32
    )
    gain_gradient = jnp.sum(norm_backward * standardized_input, axis=0)
    gain_scaled = norm_backward * norm_gain_vector
    backward_total = feature_residual.astype(jnp.float32) + inverse_deviation * (
        gain_scaled
        - jnp.mean(gain_scaled, axis=-1, keepdims=True)
        - standardized_input * jnp.mean(gain_scaled * standardized_input, axis=-1, keepdims=True)
    )
    backward_total = backward_total.astype(jnp.bfloat16)
    return (student.reshape(shape), backward_total.reshape(shape), grad_in, grad_out, gain_gradient)


def on_device(
    features, teacher, kernel_horiz, kernel_vert, norm_gain_vector, weight_in, weight_out
):
    rows_here = features.shape[0]
    cols_here = features.shape[1]
    margin = (kernel_horiz.shape[0] - 1) // 2
    parts = 2 if cols_here % 16 == 0 else 1
    width = cols_here // parts
    padded_x = extended(features, (("col", 1),), margin)
    firsts, seconds = [], []
    for k in range(parts):
        low = k * width
        first = horizontal(
            padded_x[:, low : low + width + 2 * margin], kernel_horiz, width
        ).astype(jnp.bfloat16)
        padded_first = extended(first, (("row", 0),), margin)
        firsts.append(padded_first)
        seconds.append(vertical(padded_first, kernel_vert, rows_here))
    second = jnp.concatenate(seconds, axis=1)
    student, backward_total, grad_in, grad_out, gain_gradient = pointwise(
        features, second, teacher, norm_gain_vector, weight_in, weight_out
    )
    big = lax.psum((grad_in, grad_out), ("row", "col"))
    backs, grad_vert = [], 0.0
    for k in range(parts):
        piece = backward_total[:, k * width : (k + 1) * width]
        padded_back = extended(piece, (("row", 0),), margin)
        backs.append(vertical(padded_back, kernel_vert[::-1], rows_here).astype(jnp.bfloat16))
        grad_vert = grad_vert + tap_sums(piece, firsts[k], 0)
    back_first = jnp.concatenate(backs, axis=1)
    padded_bf = extended(back_first, (("col", 1),), margin)
    grad_horiz = tap_sums(back_first, padded_x, 1)
    grad_features = (
        backward_total.astype(jnp.float32) + horizontal(padded_bf, kernel_horiz[::-1], cols_here)
    ).astype(jnp.bfloat16)
    taps = tree_sum(
        jnp.concatenate([grad_horiz, grad_vert, gain_gradient[None]], axis=0), ("col", "row")
    )
    count = grad_horiz.shape[0]
    totals = (big[0], big[1], taps[:count], taps[count : 2 * count], taps[2 * count])
    cells = rows_here * lax.axis_size("row") * cols_here * lax.axis_size("col")
    factor = 1.0 / jnp.sqrt(jnp.float32(cells))
    return (
        student,
        grad_features,
        totals[0] * factor,
        totals[1] * factor,
        totals[2] * factor,
        totals[3] * factor,
        totals[4] * factor,
    )


def solution(mesh):
    return jax.shard_map(
        on_device,
        mesh=mesh,
        in_specs=(
            P(("slab", "row"), "col", None),
            P(("slab", "row"), "col", None),
            P(),
            P(),
            P(),
            P(),
            P(),
        ),
        out_specs=(
            P(("slab", "row"), "col", None),
            P(("slab", "row"), "col", None),
            P("slab", None),
            P("slab", None),
            P("slab", None),
            P("slab", None),
            P("slab"),
        ),
        check_vma=False,
    )
```

```python
import jax
import jax.numpy as jnp
from jax import lax
from jax.sharding import PartitionSpec as P

root_half = 0.7071067811865476
inv_root_two_pi = 0.3989422804014327


def extended(x, sides, width):
    for axis, dim in sides:
        size, length = (lax.axis_size(axis), x.shape[dim])
        up = [(i, (i + 1) % size) for i in range(size - 1)]
        down = [(j, i) for i, j in up]
        last = lax.slice_in_dim(x, length - width, length, axis=dim)
        initial = lax.slice_in_dim(x, 0, width, axis=dim)
        before = lax.ppermute(last, axis, up)
        after = lax.ppermute(initial, axis, down)
        x = jnp.concatenate([before, x, after], axis=dim)
    return x


def horizontal(padded, kernel, count):
    total = jnp.zeros((padded.shape[0], count, padded.shape[2]), jnp.float32)
    for offset in range(kernel.shape[0]):
        total = total + kernel[offset] * padded[:, offset : offset + count, :]
    return total


def vertical(padded, kernel, count):
    total = jnp.zeros((count, padded.shape[1], padded.shape[2]), jnp.float32)
    for offset in range(kernel.shape[0]):
        total = total + kernel[offset] * padded[offset : offset + count, :, :]
    return total


def tap_sums(left, padded, reduce_dimension):
    length = left.shape[reduce_dimension]
    wide = left.astype(jnp.float32)
    rows_out = []
    for offset in range(padded.shape[reduce_dimension] - length + 1):
        window = lax.slice_in_dim(padded, offset, offset + length, axis=reduce_dimension)
        rows_out.append(jnp.sum(wide * window.astype(jnp.float32), axis=(0, 1)))
    return jnp.stack(rows_out)


def tree_sum(x, axes):
    for axis in axes:
        size = lax.axis_size(axis)
        if size & (size - 1):
            x = lax.psum(x, axis)
            continue
        step = 1
        while step < size:
            x = x + lax.ppermute(x, axis, [(i, i ^ step) for i in range(size)])
            step *= 2
    return x


def pointwise(features, mixed, teacher, norm_gain_vector, weight_in, weight_out):
    shape = features.shape
    chans = shape[-1]
    summed_in = features.astype(jnp.float32).reshape(-1, chans) + mixed.reshape(-1, chans)
    centre = jnp.mean(summed_in, axis=-1, keepdims=True)
    mean_removed = summed_in - centre
    spread = jnp.mean(mean_removed * mean_removed, axis=-1, keepdims=True)
    inverse_deviation = lax.rsqrt(spread + 1e-06)
    standardized_input = mean_removed * inverse_deviation
    normalized_input = (standardized_input * norm_gain_vector).astype(jnp.bfloat16)
    pre = jnp.dot(normalized_input, weight_in, preferred_element_type=jnp.float32)
    cdf = 0.5 * (1.0 + lax.erf(pre * root_half))
    activ = (pre * cdf).astype(jnp.bfloat16)
    total = summed_in + jnp.dot(activ, weight_out, preferred_element_type=jnp.float32)
    student = total.astype(jnp.bfloat16)
    feature_residual = (total - teacher.astype(jnp.float32).reshape(-1, chans)).astype(jnp.bfloat16)
    grad_out = lax.dot_general(
        activ, feature_residual, (((0,), (0,)), ((), ())), preferred_element_type=jnp.float32
    )
    back_act = lax.dot_general(
        feature_residual, weight_out, (((1,), (1,)), ((), ())), preferred_element_type=jnp.float32
    )
    slope = cdf + pre * jnp.exp(-0.5 * pre * pre) * inv_root_two_pi
    back_pre = (back_act * slope).astype(jnp.bfloat16)
    grad_in = lax.dot_general(
        normalized_input, back_pre, (((0,), (0,)), ((), ())), preferred_element_type=jnp.float32
    )
    norm_backward = lax.dot_general(
        back_pre, weight_in, (((1,), (1,)), ((), ())), preferred_element_type=jnp.float32
    )
    gain_gradient = jnp.sum(norm_backward * standardized_input, axis=0)
    gain_scaled = norm_backward * norm_gain_vector
    backward_total = feature_residual.astype(jnp.float32) + inverse_deviation * (
        gain_scaled
        - jnp.mean(gain_scaled, axis=-1, keepdims=True)
        - standardized_input * jnp.mean(gain_scaled * standardized_input, axis=-1, keepdims=True)
    )
    backward_total = backward_total.astype(jnp.bfloat16)
    return (student.reshape(shape), backward_total.reshape(shape), grad_in, grad_out, gain_gradient)


def on_device(
    features, teacher, kernel_horiz, kernel_vert, norm_gain_vector, weight_in, weight_out
):
    rows_here = features.shape[0]
    cols_here = features.shape[1]
    margin = (kernel_horiz.shape[0] - 1) // 2
    parts = 2 if cols_here % 16 == 0 else 1
    width = cols_here // parts
    padded_x = extended(features, (("col", 1),), margin)
    pieces = []
    for k in range(parts):
        low = k * width
        first = horizontal(
            padded_x[:, low : low + width + 2 * margin], kernel_horiz, width
        ).astype(jnp.bfloat16)
        padded_first = extended(first, (("row", 0),), margin)
        second = vertical(padded_first, kernel_vert, rows_here)
        student, backward_total, grad_in, grad_out, gain_gradient = pointwise(
            features[:, low : low + width],
            second,
            teacher[:, low : low + width],
            norm_gain_vector,
            weight_in,
            weight_out,
        )
        grad_vert = tap_sums(backward_total, padded_first, 0)
        padded_back = extended(backward_total, (("row", 0),), margin)
        back_first = vertical(padded_back, kernel_vert[::-1], rows_here).astype(jnp.bfloat16)
        pieces.append(
            (student, backward_total, back_first, grad_in, grad_out, gain_gradient, grad_vert)
        )
    student = jnp.concatenate([p[0] for p in pieces], axis=1)
    backward_total = jnp.concatenate([p[1] for p in pieces], axis=1)
    back_first = jnp.concatenate([p[2] for p in pieces], axis=1)
    grad_in, grad_out, gain_gradient, grad_vert = (
        sum(p[i] for p in pieces[1:]) + pieces[0][i] for i in range(3, 7)
    )
    big = lax.psum((grad_in, grad_out), ("row", "col"))
    padded_bf = extended(back_first, (("col", 1),), margin)
    grad_horiz = tap_sums(back_first, padded_x, 1)
    grad_features = (
        backward_total.astype(jnp.float32) + horizontal(padded_bf, kernel_horiz[::-1], cols_here)
    ).astype(jnp.bfloat16)
    taps = tree_sum(
        jnp.concatenate([grad_horiz, grad_vert, gain_gradient[None]], axis=0), ("col", "row")
    )
    count = grad_horiz.shape[0]
    totals = (big[0], big[1], taps[:count], taps[count : 2 * count], taps[2 * count])
    cells = rows_here * lax.axis_size("row") * cols_here * lax.axis_size("col")
    factor = 1.0 / jnp.sqrt(jnp.float32(cells))
    return (
        student,
        grad_features,
        totals[0] * factor,
        totals[1] * factor,
        totals[2] * factor,
        totals[3] * factor,
        totals[4] * factor,
    )


def solution(mesh):
    return jax.shard_map(
        on_device,
        mesh=mesh,
        in_specs=(
            P(("slab", "row"), "col", None),
            P(("slab", "row"), "col", None),
            P(),
            P(),
            P(),
            P(),
            P(),
        ),
        out_specs=(
            P(("slab", "row"), "col", None),
            P(("slab", "row"), "col", None),
            P("slab", None),
            P("slab", None),
            P("slab", None),
            P("slab", None),
            P("slab"),
        ),
        check_vma=False,
    )
```

```python
import jax
import jax.numpy as jnp
from jax import lax
from jax.sharding import PartitionSpec as P

root_half = 0.7071067811865476
inv_root_two_pi = 0.3989422804014327


def extended(x, sides, width):
    for axis, dim in sides:
        size, length = (lax.axis_size(axis), x.shape[dim])
        up = [(i, (i + 1) % size) for i in range(size - 1)]
        down = [(j, i) for i, j in up]
        last = lax.slice_in_dim(x, length - width, length, axis=dim)
        initial = lax.slice_in_dim(x, 0, width, axis=dim)
        before = lax.ppermute(last, axis, up)
        after = lax.ppermute(initial, axis, down)
        x = jnp.concatenate([before, x, after], axis=dim)
    return x


def horizontal(padded, kernel, count):
    total = jnp.zeros((padded.shape[0], count, padded.shape[2]), jnp.float32)
    for offset in range(kernel.shape[0]):
        total = total + kernel[offset] * padded[:, offset : offset + count, :]
    return total


def vertical(padded, kernel, count):
    total = jnp.zeros((count, padded.shape[1], padded.shape[2]), jnp.float32)
    for offset in range(kernel.shape[0]):
        total = total + kernel[offset] * padded[offset : offset + count, :, :]
    return total


def tap_sums(left, padded, reduce_dimension):
    length = left.shape[reduce_dimension]
    wide = left.astype(jnp.float32)
    rows_out = []
    for offset in range(padded.shape[reduce_dimension] - length + 1):
        window = lax.slice_in_dim(padded, offset, offset + length, axis=reduce_dimension)
        rows_out.append(jnp.sum(wide * window.astype(jnp.float32), axis=(0, 1)))
    return jnp.stack(rows_out)


def tree_sum(x, axes):
    for axis in axes:
        size = lax.axis_size(axis)
        if size & (size - 1):
            x = lax.psum(x, axis)
            continue
        step = 1
        while step < size:
            x = x + lax.ppermute(x, axis, [(i, i ^ step) for i in range(size)])
            step *= 2
    return x


def pointwise(features, mixed, teacher, norm_gain_vector, weight_in, weight_out):
    shape = features.shape
    chans = shape[-1]
    summed_in = features.astype(jnp.float32).reshape(-1, chans) + mixed.reshape(-1, chans)
    centre = jnp.mean(summed_in, axis=-1, keepdims=True)
    mean_removed = summed_in - centre
    spread = jnp.mean(mean_removed * mean_removed, axis=-1, keepdims=True)
    inverse_deviation = lax.rsqrt(spread + 1e-06)
    standardized_input = mean_removed * inverse_deviation
    normalized_input = (standardized_input * norm_gain_vector).astype(jnp.bfloat16)
    pre = jnp.dot(normalized_input, weight_in, preferred_element_type=jnp.float32)
    cdf = 0.5 * (1.0 + lax.erf(pre * root_half))
    activ = (pre * cdf).astype(jnp.bfloat16)
    total = summed_in + jnp.dot(activ, weight_out, preferred_element_type=jnp.float32)
    student = total.astype(jnp.bfloat16)
    feature_residual = (total - teacher.astype(jnp.float32).reshape(-1, chans)).astype(jnp.bfloat16)
    grad_out = lax.dot_general(
        activ, feature_residual, (((0,), (0,)), ((), ())), preferred_element_type=jnp.float32
    )
    back_act = lax.dot_general(
        feature_residual, weight_out, (((1,), (1,)), ((), ())), preferred_element_type=jnp.float32
    )
    slope = cdf + pre * jnp.exp(-0.5 * pre * pre) * inv_root_two_pi
    back_pre = (back_act * slope).astype(jnp.bfloat16)
    grad_in = lax.dot_general(
        normalized_input, back_pre, (((0,), (0,)), ((), ())), preferred_element_type=jnp.float32
    )
    norm_backward = lax.dot_general(
        back_pre, weight_in, (((1,), (1,)), ((), ())), preferred_element_type=jnp.float32
    )
    gain_gradient = jnp.sum(norm_backward * standardized_input, axis=0)
    gain_scaled = norm_backward * norm_gain_vector
    backward_total = feature_residual.astype(jnp.float32) + inverse_deviation * (
        gain_scaled
        - jnp.mean(gain_scaled, axis=-1, keepdims=True)
        - standardized_input * jnp.mean(gain_scaled * standardized_input, axis=-1, keepdims=True)
    )
    backward_total = backward_total.astype(jnp.bfloat16)
    return (student.reshape(shape), backward_total.reshape(shape), grad_in, grad_out, gain_gradient)


def on_device(
    features, teacher, kernel_horiz, kernel_vert, norm_gain_vector, weight_in, weight_out
):
    rows_here = features.shape[0]
    cols_here = features.shape[1]
    margin = (kernel_horiz.shape[0] - 1) // 2
    parts = 2 if cols_here % 16 == 0 else 1
    width = cols_here // parts
    padded_x = extended(features, (("col", 1),), margin)
    pieces = []
    for k in range(parts):
        low = k * width
        first = horizontal(
            padded_x[:, low : low + width + 2 * margin], kernel_horiz, width
        ).astype(jnp.bfloat16)
        padded_first = extended(first, (("row", 0),), margin)
        second = lax.optimization_barrier(vertical(padded_first, kernel_vert, rows_here))
        student, backward_total, grad_in, grad_out, gain_gradient = pointwise(
            features[:, low : low + width],
            second,
            teacher[:, low : low + width],
            norm_gain_vector,
            weight_in,
            weight_out,
        )
        grad_vert = tap_sums(backward_total, padded_first, 0)
        padded_back = extended(backward_total, (("row", 0),), margin)
        back_first = vertical(padded_back, kernel_vert[::-1], rows_here).astype(jnp.bfloat16)
        pieces.append(
            (student, backward_total, back_first, grad_in, grad_out, gain_gradient, grad_vert)
        )
    student = jnp.concatenate([p[0] for p in pieces], axis=1)
    backward_total = jnp.concatenate([p[1] for p in pieces], axis=1)
    back_first = jnp.concatenate([p[2] for p in pieces], axis=1)
    grad_in, grad_out, gain_gradient, grad_vert = (
        sum(p[i] for p in pieces[1:]) + pieces[0][i] for i in range(3, 7)
    )
    big = lax.psum((grad_in, grad_out), ("row", "col"))
    padded_bf = extended(back_first, (("col", 1),), margin)
    grad_horiz = tap_sums(back_first, padded_x, 1)
    grad_features = (
        backward_total.astype(jnp.float32) + horizontal(padded_bf, kernel_horiz[::-1], cols_here)
    ).astype(jnp.bfloat16)
    taps = tree_sum(
        jnp.concatenate([grad_horiz, grad_vert, gain_gradient[None]], axis=0), ("col", "row")
    )
    count = grad_horiz.shape[0]
    totals = (big[0], big[1], taps[:count], taps[count : 2 * count], taps[2 * count])
    cells = rows_here * lax.axis_size("row") * cols_here * lax.axis_size("col")
    factor = 1.0 / jnp.sqrt(jnp.float32(cells))
    return (
        student,
        grad_features,
        totals[0] * factor,
        totals[1] * factor,
        totals[2] * factor,
        totals[3] * factor,
        totals[4] * factor,
    )


def solution(mesh):
    return jax.shard_map(
        on_device,
        mesh=mesh,
        in_specs=(
            P(("slab", "row"), "col", None),
            P(("slab", "row"), "col", None),
            P(),
            P(),
            P(),
            P(),
            P(),
        ),
        out_specs=(
            P(("slab", "row"), "col", None),
            P(("slab", "row"), "col", None),
            P("slab", None),
            P("slab", None),
            P("slab", None),
            P("slab", None),
            P("slab"),
        ),
        check_vma=False,
    )
```

```python
import jax
import jax.numpy as jnp
from jax import lax
from jax.sharding import PartitionSpec as P

root_half = 0.7071067811865476
inv_root_two_pi = 0.3989422804014327


def extended(x, sides, width):
    for axis, dim in sides:
        size, length = (lax.axis_size(axis), x.shape[dim])
        up = [(i, (i + 1) % size) for i in range(size - 1)]
        down = [(j, i) for i, j in up]
        last = lax.slice_in_dim(x, length - width, length, axis=dim)
        initial = lax.slice_in_dim(x, 0, width, axis=dim)
        before = lax.ppermute(last, axis, up)
        after = lax.ppermute(initial, axis, down)
        x = jnp.concatenate([before, x, after], axis=dim)
    return x


def horizontal(padded, kernel, count):
    total = jnp.zeros((padded.shape[0], count, padded.shape[2]), jnp.float32)
    for offset in range(kernel.shape[0]):
        total = total + kernel[offset] * padded[:, offset : offset + count, :]
    return total


def vertical(padded, kernel, count):
    total = jnp.zeros((count, padded.shape[1], padded.shape[2]), jnp.float32)
    for offset in range(kernel.shape[0]):
        total = total + kernel[offset] * padded[offset : offset + count, :, :]
    return total


def tap_sums(left, padded, reduce_dimension):
    length = left.shape[reduce_dimension]
    wide = left.astype(jnp.float32)
    rows_out = []
    for offset in range(padded.shape[reduce_dimension] - length + 1):
        window = lax.slice_in_dim(padded, offset, offset + length, axis=reduce_dimension)
        rows_out.append(jnp.sum(wide * window.astype(jnp.float32), axis=(0, 1)))
    return jnp.stack(rows_out)


def tree_sum(x, axes):
    for axis in axes:
        size = lax.axis_size(axis)
        if size & (size - 1):
            x = lax.psum(x, axis)
            continue
        step = 1
        while step < size:
            x = x + lax.ppermute(x, axis, [(i, i ^ step) for i in range(size)])
            step *= 2
    return x


def pointwise(features, mixed, teacher, norm_gain_vector, weight_in, weight_out):
    shape = features.shape
    chans = shape[-1]
    summed_in = features.astype(jnp.float32).reshape(-1, chans) + mixed.reshape(-1, chans)
    centre = jnp.mean(summed_in, axis=-1, keepdims=True)
    mean_removed = summed_in - centre
    spread = jnp.mean(mean_removed * mean_removed, axis=-1, keepdims=True)
    inverse_deviation = lax.rsqrt(spread + 1e-06)
    standardized_input = mean_removed * inverse_deviation
    normalized_input = (standardized_input * norm_gain_vector).astype(jnp.bfloat16)
    pre = jnp.dot(normalized_input, weight_in, preferred_element_type=jnp.float32)
    cdf = 0.5 * (1.0 + lax.erf(pre * root_half))
    activ = (pre * cdf).astype(jnp.bfloat16)
    total = summed_in + jnp.dot(activ, weight_out, preferred_element_type=jnp.float32)
    student = total.astype(jnp.bfloat16)
    feature_residual = (total - teacher.astype(jnp.float32).reshape(-1, chans)).astype(jnp.bfloat16)
    grad_out = lax.dot_general(
        activ, feature_residual, (((0,), (0,)), ((), ())), preferred_element_type=jnp.float32
    )
    back_act = lax.dot_general(
        feature_residual, weight_out, (((1,), (1,)), ((), ())), preferred_element_type=jnp.float32
    )
    slope = cdf + pre * jnp.exp(-0.5 * pre * pre) * inv_root_two_pi
    back_pre = (back_act * slope).astype(jnp.bfloat16)
    grad_in = lax.dot_general(
        normalized_input, back_pre, (((0,), (0,)), ((), ())), preferred_element_type=jnp.float32
    )
    norm_backward = lax.dot_general(
        back_pre, weight_in, (((1,), (1,)), ((), ())), preferred_element_type=jnp.float32
    )
    gain_gradient = jnp.sum(norm_backward * standardized_input, axis=0)
    gain_scaled = norm_backward * norm_gain_vector
    backward_total = feature_residual.astype(jnp.float32) + inverse_deviation * (
        gain_scaled
        - jnp.mean(gain_scaled, axis=-1, keepdims=True)
        - standardized_input * jnp.mean(gain_scaled * standardized_input, axis=-1, keepdims=True)
    )
    backward_total = backward_total.astype(jnp.bfloat16)
    return (student.reshape(shape), backward_total.reshape(shape), grad_in, grad_out, gain_gradient)


def on_device(
    features, teacher, kernel_horiz, kernel_vert, norm_gain_vector, weight_in, weight_out
):
    rows_here = features.shape[0]
    cols_here = features.shape[1]
    margin = (kernel_horiz.shape[0] - 1) // 2
    parts = 2 if cols_here % 16 == 0 else 1
    width = cols_here // parts
    padded_x = extended(features, (("col", 1),), margin)
    pieces = []
    for k in range(parts):
        low = k * width
        first = horizontal(
            padded_x[:, low : low + width + 2 * margin], kernel_horiz, width
        ).astype(jnp.bfloat16)
        padded_first = extended(first, (("row", 0),), margin)
        if pieces:
            padded_first, pieces[-1][1] = lax.optimization_barrier((padded_first, pieces[-1][1]))
        second = lax.optimization_barrier(vertical(padded_first, kernel_vert, rows_here))
        student, backward_total, grad_in, grad_out, gain_gradient = pointwise(
            features[:, low : low + width],
            second,
            teacher[:, low : low + width],
            norm_gain_vector,
            weight_in,
            weight_out,
        )
        grad_vert = tap_sums(backward_total, padded_first, 0)
        padded_back = extended(backward_total, (("row", 0),), margin)
        back_first = vertical(padded_back, kernel_vert[::-1], rows_here).astype(jnp.bfloat16)
        pieces.append(
            [student, backward_total, back_first, grad_in, grad_out, gain_gradient, grad_vert]
        )
    student = jnp.concatenate([p[0] for p in pieces], axis=1)
    backward_total = jnp.concatenate([p[1] for p in pieces], axis=1)
    back_first = jnp.concatenate([p[2] for p in pieces], axis=1)
    grad_in, grad_out, gain_gradient, grad_vert = (
        sum(p[i] for p in pieces[1:]) + pieces[0][i] for i in range(3, 7)
    )
    big = lax.psum((grad_in, grad_out), ("row", "col"))
    padded_bf = extended(back_first, (("col", 1),), margin)
    grad_horiz = tap_sums(back_first, padded_x, 1)
    grad_features = (
        backward_total.astype(jnp.float32) + horizontal(padded_bf, kernel_horiz[::-1], cols_here)
    ).astype(jnp.bfloat16)
    taps = tree_sum(
        jnp.concatenate([grad_horiz, grad_vert, gain_gradient[None]], axis=0), ("col", "row")
    )
    count = grad_horiz.shape[0]
    totals = (big[0], big[1], taps[:count], taps[count : 2 * count], taps[2 * count])
    cells = rows_here * lax.axis_size("row") * cols_here * lax.axis_size("col")
    factor = 1.0 / jnp.sqrt(jnp.float32(cells))
    return (
        student,
        grad_features,
        totals[0] * factor,
        totals[1] * factor,
        totals[2] * factor,
        totals[3] * factor,
        totals[4] * factor,
    )


def solution(mesh):
    return jax.shard_map(
        on_device,
        mesh=mesh,
        in_specs=(
            P(("slab", "row"), "col", None),
            P(("slab", "row"), "col", None),
            P(),
            P(),
            P(),
            P(),
            P(),
        ),
        out_specs=(
            P(("slab", "row"), "col", None),
            P(("slab", "row"), "col", None),
            P("slab", None),
            P("slab", None),
            P("slab", None),
            P("slab", None),
            P("slab"),
        ),
        check_vma=False,
    )
```
